256 devices in a mesh: ctx: 32 (over x, z), head: 8 (over y, core).
Axes of the slice: x: 4, y: 4, z: 8, core: 2. Of those that a mesh axis runs over, the one named last changes fastest.
Arguments:
- query_in: bfloat16 [16384, 2048], P('ctx', 'head'), may hold values from -6 to 6
- key_in: bfloat16 [16384, 2048], P('ctx', 'head'), may hold values from -6 to 6
- value_in: bfloat16 [16384, 4096], P('ctx', 'head'), may hold values from -6 to 6
- query_taps: float32 [4, 2048], P(None, 'head'), may hold values from -3 to 3
- key_taps: float32 [4, 2048], P(None, 'head'), may hold values from -3 to 3
- value_taps: float32 [4, 4096], P(None, 'head'), may hold values from -3 to 3
- log_decay: float32 [32, 16384], P('head', 'ctx'), may hold values from -2 to 0
- beta_logit: float32 [32, 16384], P('head', 'ctx'), may hold values from -9 to 2
- gate_in: bfloat16 [16384, 4096], P('ctx', 'head'), may hold values from -6 to 6
- norm_gain: float32 [128], replicated, may hold values from 0.1 to 1.9
Outputs:
- core_out: bfloat16 [16384, 4096], P(('ctx', 'head'))
The draws below stay inside these ranges and needn't reach their ends.
All inputs are finite; a program needn't handle non-finite values.
Results may differ from the reference program's by a relative error of at most 0.005.
Values may be sent and summed in bfloat16 or wider, within the bound.
No kernel may reach another device: no remote copies, remote signals or barrier semaphores. Data moves between devices by JAX's collectives and lax.ppermute only.
A program may use at most 64 MiB of HBM per device.

```python
import jax
import jax.numpy as jnp
from jax import lax

DK = 128
KH = 16
OUTPUT_CHANNELS = 32
CONV = 4
GROUP = 64
TOK_DEV = 512
INPUT_LENGTH = 16384


def head_kinds(key):
    share = 0.5
    return jax.random.bernoulli(jax.random.fold_in(key, 11), share, (OUTPUT_CHANNELS,))


def draw_log_decay(key, part):
    lagging_channels = head_kinds(key)
    block_count = INPUT_LENGTH // TOK_DEV
    block_factor = jnp.exp(jax.random.uniform(jax.random.fold_in(key, 21), (OUTPUT_CHANNELS, block_count), jnp.float32, -0.7, 0.7))
    factor = jnp.repeat(block_factor, TOK_DEV, axis=1)
    rough = jnp.exp(jax.random.uniform(jax.random.fold_in(key, 22), (OUTPUT_CHANNELS, INPUT_LENGTH), jnp.float32, -0.7, 0.7))
    fast_rate = rough * factor / 40.0
    slow_rate = rough * factor * 0.8 / INPUT_LENGTH
    forgetting_speed = jnp.where(lagging_channels[:, None], slow_rate, fast_rate)
    sequence_indices = jax.random.randint(jax.random.fold_in(key, 23), (OUTPUT_CHANNELS, 3), 0, INPUT_LENGTH)
    kept_fraction = jax.random.uniform(jax.random.fold_in(key, 24), (OUTPUT_CHANNELS, 3), jnp.float32, 0.6, 0.8)
    lines_by_channel = jnp.broadcast_to(jnp.arange(OUTPUT_CHANNELS)[:, None], (OUTPUT_CHANNELS, 3))
    spike_clusters = jnp.zeros((OUTPUT_CHANNELS, INPUT_LENGTH), jnp.float32).at[lines_by_channel, sequence_indices].add(jnp.log(kept_fraction))
    spike_clusters = jnp.where(lagging_channels[:, None], spike_clusters, 0.0)
    return (spike_clusters - forgetting_speed).astype(jnp.float32)


def draw_beta_logit(key, part):
    lagging_channels = head_kinds(key)
    rough = jnp.exp(jax.random.uniform(jax.random.fold_in(key, 31), (OUTPUT_CHANNELS, INPUT_LENGTH), jnp.float32, -0.7, 0.7))
    fast_logit = jnp.clip(jax.random.normal(jax.random.fold_in(key, 32), (OUTPUT_CHANNELS, INPUT_LENGTH), jnp.float32), -2.0, 2.0)
    small = jnp.minimum(38.0 / INPUT_LENGTH * rough, 0.5)
    slow_logit = jnp.log(small) - jnp.log1p(-small)
    return jnp.where(lagging_channels[:, None], slow_logit, fast_logit).astype(jnp.float32)


def level_of(stream_key, shape, cuts, low, high):
    level = 1.0
    for dim, shards_of in cuts:
        steps = jax.random.uniform(jax.random.fold_in(jax.random.fold_in(stream_key, 6), dim), (shards_of,), jnp.float32, low / len(cuts), high / len(cuts))
        level = level * jnp.repeat(jnp.exp(steps), shape[dim] // shards_of).reshape((-1,) + (1,) * (len(shape) - 1 - dim))
    return level


def bell_draw(stream_key, dims, deviation, reach, pieces=(), kind=jnp.bfloat16):
    entries = deviation * jax.random.normal(stream_key, dims, jnp.float32)
    if pieces:
        entries = entries * level_of(stream_key, dims, pieces, -0.22, 0.18)
    return jnp.clip(entries, -reach, reach).astype(kind)


def setup_inputs(seed: int = 0) -> dict:
    key_of = jax.random.split(jax.random.key(seed), 11)
    query_in = bell_draw(key_of[0], (INPUT_LENGTH, KH * DK), 1.0, 6.0, ((0, 32), (1, 8)))
    key_in = bell_draw(key_of[1], (INPUT_LENGTH, KH * DK), 1.0, 6.0, ((0, 32), (1, 8)))
    value_in = bell_draw(key_of[2], (INPUT_LENGTH, OUTPUT_CHANNELS * DK), 1.0, 6.0, ((0, 32), (1, 8)))
    query_taps = bell_draw(key_of[3], (CONV, KH * DK), CONV ** -0.5, 3.0, ((1, 8),), jnp.float32)
    key_taps = bell_draw(key_of[4], (CONV, KH * DK), CONV ** -0.5, 3.0, ((1, 8),), jnp.float32)
    value_taps = bell_draw(key_of[5], (CONV, OUTPUT_CHANNELS * DK), CONV ** -0.5, 3.0, ((1, 8),), jnp.float32)
    log_decay = draw_log_decay(jax.random.fold_in(key_of[10], 71), 0)
    beta_logit = draw_beta_logit(jax.random.fold_in(key_of[10], 71), 0)
    gate_in = bell_draw(key_of[8], (INPUT_LENGTH, OUTPUT_CHANNELS * DK), 1.0, 6.0, ((0, 32), (1, 8)))
    norm_gain = jnp.clip(1.0 + 0.18 * jax.random.normal(key_of[9], (DK,), jnp.float32), 0.1, 1.9)
    return {"query_in": query_in, "key_in": key_in, "value_in": value_in, "query_taps": query_taps, "key_taps": key_taps, "value_taps": value_taps, "log_decay": log_decay, "beta_logit": beta_logit, "gate_in": gate_in, "norm_gain": norm_gain}


highest = lax.Precision.HIGHEST
norm_eps = 1e-06

def causal_conv(joined, taps, length):
    weights = taps.astype(jnp.float32)
    summed = jnp.zeros((length, joined.shape[1]), jnp.float32)
    for offset in range(weights.shape[0]):
        summed = summed + weights[offset] * joined[offset:offset + length].astype(jnp.float32)
    return jax.nn.silu(summed)

def unit_rows(matrix):
    return matrix * lax.rsqrt(lax.optimization_barrier(jnp.sum(matrix * matrix, axis=-1, keepdims=True)) + norm_eps)

def group_terms(query, keys, values, beta, logdecay):
    length = logdecay.shape[-1]
    cumul = jnp.cumsum(logdecay, axis=-1)
    row_ids = lax.broadcasted_iota(jnp.int32, (length, length), 0)
    col_ids = lax.broadcasted_iota(jnp.int32, (length, length), 1)
    inside = col_ids <= row_ids
    differ = cumul[..., :, None] - cumul[..., None, :]
    decay_mask = jnp.where(inside, jnp.exp(jnp.where(inside, differ, 0.0)), 0.0)
    keygram = jnp.einsum('...ik,...jk->...ij', keys, keys, precision=highest)
    strict = jnp.where(col_ids < row_ids, beta[..., :, None] * keygram * decay_mask, 0.0)
    identity_mats = jnp.broadcast_to(jnp.eye(length, dtype=jnp.float32), strict.shape)
    inverse = lax.linalg.triangular_solve(identity_mats + strict, identity_mats, left_side=True, lower=True, unit_diagonal=True)
    upd_values = jnp.einsum('...ij,...jd->...id', inverse, beta[..., None] * values, precision=highest)
    upd_keys = jnp.einsum('...ij,...jd->...id', inverse, (beta * jnp.exp(cumul))[..., None] * keys, precision=highest)
    scores = jnp.einsum('...ik,...jk->...ij', query, keys, precision=highest) * decay_mask
    last_log = cumul[..., -1:]
    query_decay = query * jnp.exp(cumul)[..., None]
    key_decay = keys * jnp.exp(last_log - cumul)[..., None]
    return (upd_values, upd_keys, scores, query_decay, key_decay, last_log[..., 0])

def group_step(state, terms):
    upd_values, upd_keys, scores, query_decay, key_decay, last_log = terms
    new_values = upd_values - jnp.einsum('...ik,...kd->...id', upd_keys, state, precision=highest)
    output = jnp.einsum('...ik,...kd->...id', query_decay, state, precision=highest)
    output = output + jnp.einsum('...ij,...jd->...id', scores, new_values, precision=highest)
    state = jnp.exp(last_log)[..., None, None] * state + jnp.einsum('...ik,...id->...kd', key_decay, new_values, precision=highest)
    return (state, output)

def reference(query_in, key_in, value_in, query_taps, key_taps, value_taps, log_decay, beta_logit, gate_in, norm_gain):
    tokens_all = query_in.shape[0]
    rim_width = CONV - 1

    def padded(inputs):
        return jnp.concatenate([jnp.zeros((rim_width, inputs.shape[1]), jnp.bfloat16), inputs], axis=0)
    query_conv = causal_conv(padded(query_in), query_taps, tokens_all)
    key_conv = causal_conv(padded(key_in), key_taps, tokens_all)
    value_conv = causal_conv(padded(value_in), value_taps, tokens_all)
    queries = (unit_rows(query_conv.reshape(tokens_all, KH, DK)) * DK ** (-0.5)).astype(jnp.bfloat16)
    keys = unit_rows(key_conv.reshape(tokens_all, KH, DK)).astype(jnp.bfloat16)
    values = value_conv.reshape(tokens_all, OUTPUT_CHANNELS, DK).astype(jnp.bfloat16)
    beta = jax.nn.sigmoid(beta_logit)
    gates = gate_in.reshape(tokens_all, OUTPUT_CHANNELS, DK)
    groups_all = tokens_all // GROUP

    def per_head(head_index):
        key_index = head_index // (OUTPUT_CHANNELS // KH)
        query_head = lax.dynamic_index_in_dim(queries, key_index, 1, keepdims=False).astype(jnp.float32).reshape(groups_all, GROUP, DK)
        key_head = lax.dynamic_index_in_dim(keys, key_index, 1, keepdims=False).astype(jnp.float32).reshape(groups_all, GROUP, DK)
        value_head = lax.dynamic_index_in_dim(values, head_index, 1, keepdims=False).astype(jnp.float32).reshape(groups_all, GROUP, DK)
        beta_head = lax.dynamic_index_in_dim(beta, head_index, 0, keepdims=False).reshape(groups_all, GROUP)
        decay_head = lax.dynamic_index_in_dim(log_decay, head_index, 0, keepdims=False).reshape(groups_all, GROUP)
        terms = group_terms(query_head, key_head, value_head, beta_head, decay_head)
        _, outputs = lax.scan(group_step, jnp.zeros((DK, DK), jnp.float32), terms)
        output = outputs.reshape(tokens_all, DK)
        gate = lax.dynamic_index_in_dim(gates, head_index, 1, keepdims=False).astype(jnp.float32)
        normed = output * lax.rsqrt(lax.optimization_barrier(jnp.mean(output * output, axis=-1, keepdims=True)) + norm_eps) * norm_gain * jax.nn.silu(gate)
        return normed.astype(jnp.bfloat16)
    stacked = lax.map(per_head, jnp.arange(OUTPUT_CHANNELS, dtype=jnp.int32))
    return stacked.transpose(1, 0, 2).reshape(tokens_all, OUTPUT_CHANNELS * DK)
```

```python
import jax
import jax.numpy as jnp
from jax import lax
from jax.sharding import PartitionSpec as P

GROUP = 64


highest = lax.Precision.HIGHEST
norm_eps = 1e-06


def shifted(value, axis, steps):
    count = lax.axis_size(axis)
    first, last = (max(0, -steps), min(count, count - steps))
    return lax.ppermute(value, axis, [(source, source + steps) for source in range(first, last)])


def causal_conv(joined, taps, length):
    summed = jnp.zeros((length, joined.shape[1]), jnp.float32)
    for offset in range(taps.shape[0]):
        summed = summed + taps[offset] * joined[offset : offset + length].astype(jnp.float32)
    return jax.nn.silu(summed)


def unit_rows(matrix):
    return matrix * lax.rsqrt(jnp.sum(matrix * matrix, axis=-1, keepdims=True) + norm_eps)


def unit_lower_inverse(strict, row_ids, col_ids):
    length = strict.shape[-1]
    eye = (row_ids == col_ids).astype(jnp.float32)
    inverse = eye - jnp.where(row_ids // 2 == col_ids // 2, strict, 0.0)

    def level(depth, inverse):
        width = 2 << depth
        lower_left = jnp.where(
            (row_ids // (2 * width) == col_ids // (2 * width)) & (row_ids // width != col_ids // width),
            strict,
            0.0,
        )
        return inverse - matmul_pair(matmul_pair(inverse, lower_left), inverse)

    return lax.fori_loop(0, length.bit_length() - 2, level, inverse)


def group_terms(query, keys, values, beta, logdecay):
    length = logdecay.shape[-1]
    cumul = jnp.cumsum(logdecay, axis=-1)
    row_ids = lax.broadcasted_iota(jnp.int32, (length, length), 0)
    col_ids = lax.broadcasted_iota(jnp.int32, (length, length), 1)
    inside = col_ids <= row_ids
    differ = cumul[..., :, None] - cumul[..., None, :]
    decay_mask = jnp.where(inside, jnp.exp(jnp.where(inside, differ, 0.0)), 0.0)
    keygram = jnp.einsum("...ik,...jk->...ij", keys, keys, precision=highest)
    strict = jnp.where(col_ids < row_ids, beta[..., :, None] * keygram * decay_mask, 0.0)
    inverse = unit_lower_inverse(strict, row_ids, col_ids)
    upd_values = jnp.einsum(
        "...ij,...jd->...id", inverse, beta[..., None] * values, precision=highest
    )
    upd_keys = jnp.einsum(
        "...ij,...jd->...id", inverse, (beta * jnp.exp(cumul))[..., None] * keys, precision=highest
    )
    scores = jnp.einsum("...ik,...jk->...ij", query, keys, precision=highest) * decay_mask
    last_log = cumul[..., -1:]
    query_decay = query * jnp.exp(cumul)[..., None]
    key_decay = keys * jnp.exp(last_log - cumul)[..., None]
    return (upd_values, upd_keys, scores, query_decay, key_decay, last_log[..., 0])


def group_step(state, terms):
    upd_values, upd_keys, scores, query_decay, key_decay, last_log = terms
    new_values = upd_values - jnp.einsum("...ik,...kd->...id", upd_keys, state, precision=highest)
    output = jnp.einsum("...ik,...kd->...id", query_decay, state, precision=highest)
    output = output + jnp.einsum("...ij,...jd->...id", scores, new_values, precision=highest)
    state = jnp.exp(last_log)[..., None, None] * state + jnp.einsum(
        "...ik,...id->...kd", key_decay, new_values, precision=highest
    )
    return (state, output)


def matmul_pair(left_mats, right_mats):
    return jnp.einsum("...ij,...jk->...ik", left_mats, right_mats, precision=highest)


def body(
    query_in,
    key_in,
    value_in,
    query_taps,
    key_taps,
    value_taps,
    log_decay,
    beta_logit,
    gate_in,
    norm_gain,
):
    head_size = norm_gain.shape[0]
    length = query_in.shape[0]
    value_heads = log_decay.shape[0]
    key_heads = query_in.shape[1] // head_size
    share_ratio = value_heads // key_heads
    rim_width = query_taps.shape[0] - 1
    groups_dev = length // GROUP
    tail_rows = shifted(
        (
            query_in[length - rim_width :],
            key_in[length - rim_width :],
            value_in[length - rim_width :],
        ),
        "ctx",
        1,
    )
    query_conv = causal_conv(jnp.concatenate([tail_rows[0], query_in], axis=0), query_taps, length)
    key_conv = causal_conv(jnp.concatenate([tail_rows[1], key_in], axis=0), key_taps, length)
    value_conv = causal_conv(jnp.concatenate([tail_rows[2], value_in], axis=0), value_taps, length)
    queries = (
        unit_rows(query_conv.reshape(length, key_heads, head_size)) * head_size ** (-0.5)
    ).astype(jnp.bfloat16)
    keys = unit_rows(key_conv.reshape(length, key_heads, head_size)).astype(jnp.bfloat16)
    values = value_conv.reshape(length, value_heads, head_size).astype(jnp.bfloat16)

    def blocked(array):
        return (
            array.astype(jnp.float32)
            .reshape(groups_dev, GROUP, array.shape[1], head_size)
            .transpose(0, 2, 1, 3)
        )

    def blocked_rates(array):
        return array.reshape(value_heads, groups_dev, GROUP).transpose(1, 0, 2)

    query_blocks = blocked(jnp.repeat(queries, share_ratio, axis=1))
    key_blocks = blocked(jnp.repeat(keys, share_ratio, axis=1))
    value_blocks = blocked(values)
    beta_blocks = blocked_rates(jax.nn.sigmoid(beta_logit))
    decay_blocks = blocked_rates(log_decay)
    terms = group_terms(query_blocks, key_blocks, value_blocks, beta_blocks, decay_blocks)
    upd_values, upd_keys, scores, query_decay, key_decay, last_log = terms
    identity_state = jnp.broadcast_to(
        jnp.eye(head_size, dtype=jnp.float32), (value_heads, head_size, head_size)
    )
    group_maps = jnp.exp(last_log)[..., None, None] * identity_state - jnp.einsum(
        "...ik,...ij->...kj", key_decay, upd_keys, precision=highest
    )
    query_effect = query_decay - matmul_pair(scores, upd_keys)

    def local_step(carry, packed):
        state, product = carry
        group, group_map = packed
        state, output = group_step(state, group)
        return ((state, matmul_pair(group_map, product)), output)

    zero_state = jnp.zeros((value_heads, head_size, head_size), jnp.float32)
    (local_state, shard_map_mat), local_out = lax.scan(
        local_step, (zero_state, identity_state), (terms, group_maps)
    )

    ctx_count = lax.axis_size("ctx")
    span_map, span_state = shard_map_mat, local_state
    reach = 1
    while reach < ctx_count:
        if 2 * reach < ctx_count:
            prior_map, prior_state = shifted((span_map, span_state), "ctx", reach)
            span_state = matmul_pair(span_map, prior_state) + span_state
            span_map = matmul_pair(span_map, prior_map)
        else:
            prior_state = shifted(span_state, "ctx", reach)
            span_state = matmul_pair(span_map, prior_state) + span_state
        reach *= 2
    incoming = shifted(span_state, "ctx", 1)

    def carried_step(state, packed):
        effect_group, group_map = packed
        return (matmul_pair(group_map, state), matmul_pair(effect_group, state))

    _, carried_out = lax.scan(carried_step, incoming, (query_effect, group_maps))
    output = (local_out + carried_out).transpose(0, 2, 1, 3).reshape(length, value_heads, head_size)
    gates = gate_in.reshape(length, value_heads, head_size).astype(jnp.float32)
    normed = (
        output
        * lax.rsqrt(jnp.mean(output * output, axis=-1, keepdims=True) + norm_eps)
        * norm_gain
        * jax.nn.silu(gates)
    )
    normed = normed.astype(jnp.bfloat16).reshape(length, value_heads * head_size)
    return lax.all_to_all(normed, "head", split_axis=0, concat_axis=1, tiled=True)


def solution(mesh):
    in_specs = (
        P("ctx", "head"),
        P("ctx", "head"),
        P("ctx", "head"),
        P(None, "head"),
        P(None, "head"),
        P(None, "head"),
        P("head", "ctx"),
        P("head", "ctx"),
        P("ctx", "head"),
        P(),
    )
    out_specs = P(("ctx", "head"), None)
    return jax.shard_map(body, mesh=mesh, in_specs=in_specs, out_specs=out_specs, check_vma=False)
```

```python
import jax
import jax.numpy as jnp
from jax import lax
from jax.sharding import PartitionSpec as P

GROUP = 64


highest = lax.Precision.HIGHEST
norm_eps = 1e-06


def shifted(value, axis, steps):
    count = lax.axis_size(axis)
    first, last = (max(0, -steps), min(count, count - steps))
    return lax.ppermute(value, axis, [(source, source + steps) for source in range(first, last)])


def causal_conv(joined, taps, length):
    summed = jnp.zeros((length, joined.shape[1]), jnp.float32)
    for offset in range(taps.shape[0]):
        summed = summed + taps[offset] * joined[offset : offset + length].astype(jnp.float32)
    return jax.nn.silu(summed)


def unit_rows(matrix):
    return matrix * lax.rsqrt(jnp.sum(matrix * matrix, axis=-1, keepdims=True) + norm_eps)


def unit_lower_inverse(strict, row_ids, col_ids):
    length = strict.shape[-1]
    eye = (row_ids == col_ids).astype(jnp.float32)
    inverse = eye - jnp.where(row_ids // 2 == col_ids // 2, strict, 0.0)

    def level(depth, inverse):
        width = 2 << depth
        lower_left = jnp.where(
            (row_ids // (2 * width) == col_ids // (2 * width)) & (row_ids // width != col_ids // width),
            strict,
            0.0,
        )
        return inverse - matmul_pair(matmul_pair(inverse, lower_left), inverse)

    return lax.fori_loop(0, length.bit_length() - 2, level, inverse)


def group_terms(query, keys, values, beta, logdecay):
    length = logdecay.shape[-1]
    cumul = jnp.cumsum(logdecay, axis=-1)
    row_ids = lax.broadcasted_iota(jnp.int32, (length, length), 0)
    col_ids = lax.broadcasted_iota(jnp.int32, (length, length), 1)
    inside = col_ids <= row_ids
    differ = cumul[..., :, None] - cumul[..., None, :]
    decay_mask = jnp.where(inside, jnp.exp(jnp.where(inside, differ, 0.0)), 0.0)
    keygram = jnp.einsum("...ik,...jk->...ij", keys, keys, precision=highest)
    strict = jnp.where(col_ids < row_ids, beta[..., :, None] * keygram * decay_mask, 0.0)
    inverse = unit_lower_inverse(strict, row_ids, col_ids)
    upd_values = jnp.einsum(
        "...ij,...jd->...id", inverse, beta[..., None] * values, precision=highest
    )
    upd_keys = jnp.einsum(
        "...ij,...jd->...id", inverse, (beta * jnp.exp(cumul))[..., None] * keys, precision=highest
    )
    scores = jnp.einsum("...ik,...jk->...ij", query, keys, precision=highest) * decay_mask
    last_log = cumul[..., -1:]
    query_decay = query * jnp.exp(cumul)[..., None]
    key_decay = keys * jnp.exp(last_log - cumul)[..., None]
    return (upd_values, upd_keys, scores, query_decay, key_decay, last_log[..., 0])


def group_step(state, terms):
    upd_values, upd_keys, scores, query_decay, key_decay, last_log = terms
    new_values = upd_values - jnp.einsum("...ik,...kd->...id", upd_keys, state, precision=highest)
    output = jnp.einsum("...ik,...kd->...id", query_decay, state, precision=highest)
    output = output + jnp.einsum("...ij,...jd->...id", scores, new_values, precision=highest)
    state = jnp.exp(last_log)[..., None, None] * state + jnp.einsum(
        "...ik,...id->...kd", key_decay, new_values, precision=highest
    )
    return (state, output)


def matmul_pair(left_mats, right_mats):
    return jnp.einsum("...ij,...jk->...ik", left_mats, right_mats, precision=highest)


def body(
    query_in,
    key_in,
    value_in,
    query_taps,
    key_taps,
    value_taps,
    log_decay,
    beta_logit,
    gate_in,
    norm_gain,
):
    head_size = norm_gain.shape[0]
    length = query_in.shape[0]
    value_heads = log_decay.shape[0]
    key_heads = query_in.shape[1] // head_size
    share_ratio = value_heads // key_heads
    rim_width = query_taps.shape[0] - 1
    groups_dev = length // GROUP
    tail_rows = shifted(
        (
            query_in[length - rim_width :],
            key_in[length - rim_width :],
            value_in[length - rim_width :],
        ),
        "ctx",
        1,
    )
    query_conv = causal_conv(jnp.concatenate([tail_rows[0], query_in], axis=0), query_taps, length)
    key_conv = causal_conv(jnp.concatenate([tail_rows[1], key_in], axis=0), key_taps, length)
    value_conv = causal_conv(jnp.concatenate([tail_rows[2], value_in], axis=0), value_taps, length)
    queries = (
        unit_rows(query_conv.reshape(length, key_heads, head_size)) * head_size ** (-0.5)
    ).astype(jnp.bfloat16)
    keys = unit_rows(key_conv.reshape(length, key_heads, head_size)).astype(jnp.bfloat16)
    values = value_conv.reshape(length, value_heads, head_size).astype(jnp.bfloat16)

    def blocked(array):
        return (
            array.astype(jnp.float32)
            .reshape(groups_dev, GROUP, array.shape[1], head_size)
            .transpose(0, 2, 1, 3)
        )

    def blocked_rates(array):
        return array.reshape(value_heads, groups_dev, GROUP).transpose(1, 0, 2)

    query_blocks = blocked(jnp.repeat(queries, share_ratio, axis=1))
    key_blocks = blocked(jnp.repeat(keys, share_ratio, axis=1))
    value_blocks = blocked(values)
    beta_blocks = blocked_rates(jax.nn.sigmoid(beta_logit))
    decay_blocks = blocked_rates(log_decay)
    terms = group_terms(query_blocks, key_blocks, value_blocks, beta_blocks, decay_blocks)
    upd_values, upd_keys, scores, query_decay, key_decay, last_log = terms
    identity_state = jnp.broadcast_to(
        jnp.eye(head_size, dtype=jnp.float32), (value_heads, head_size, head_size)
    )
    group_maps = jnp.exp(last_log)[..., None, None] * identity_state - jnp.einsum(
        "...ik,...ij->...kj", key_decay, upd_keys, precision=highest
    )
    group_offsets = jnp.einsum("...ik,...id->...kd", key_decay, upd_values, precision=highest)
    query_effect = query_decay - matmul_pair(scores, upd_keys)
    zero_state = jnp.zeros((value_heads, head_size, head_size), jnp.float32)

    span_maps, span_offsets = group_maps, group_offsets
    reach = 1
    while reach < groups_dev:
        prior_maps = jnp.concatenate(
            [jnp.broadcast_to(identity_state, (reach,) + identity_state.shape), span_maps[: groups_dev - reach]]
        )
        prior_offsets = jnp.concatenate(
            [jnp.broadcast_to(zero_state, (reach,) + zero_state.shape), span_offsets[: groups_dev - reach]]
        )
        span_offsets = matmul_pair(span_maps, prior_offsets) + span_offsets
        span_maps = matmul_pair(span_maps, prior_maps)
        reach *= 2
    shard_map_mat, local_state = span_maps[-1], span_offsets[-1]
    entry_maps = jnp.concatenate([identity_state[None], span_maps[:-1]])
    entry_offsets = jnp.concatenate([zero_state[None], span_offsets[:-1]])
    state_effect = matmul_pair(query_effect, entry_maps)
    local_out = matmul_pair(query_effect, entry_offsets) + matmul_pair(scores, upd_values)

    ctx_count = lax.axis_size("ctx")
    span_map, span_state = shard_map_mat, local_state
    reach = 1
    while reach < ctx_count:
        if 2 * reach < ctx_count:
            prior_map, prior_state = shifted((span_map, span_state), "ctx", reach)
            span_state = matmul_pair(span_map, prior_state) + span_state
            span_map = matmul_pair(span_map, prior_map)
        else:
            prior_state = shifted(span_state, "ctx", reach)
            span_state = matmul_pair(span_map, prior_state) + span_state
        reach *= 2
    incoming = shifted(span_state, "ctx", 1)

    carried_out = jnp.einsum("ghik,hkd->ghid", state_effect, incoming, precision=highest)
    output = (local_out + carried_out).transpose(0, 2, 1, 3).reshape(length, value_heads, head_size)
    gates = gate_in.reshape(length, value_heads, head_size).astype(jnp.float32)
    normed = (
        output
        * lax.rsqrt(jnp.mean(output * output, axis=-1, keepdims=True) + norm_eps)
        * norm_gain
        * jax.nn.silu(gates)
    )
    normed = normed.astype(jnp.bfloat16).reshape(length, value_heads * head_size)
    return lax.all_to_all(normed, "head", split_axis=0, concat_axis=1, tiled=True)


def solution(mesh):
    in_specs = (
        P("ctx", "head"),
        P("ctx", "head"),
        P("ctx", "head"),
        P(None, "head"),
        P(None, "head"),
        P(None, "head"),
        P("head", "ctx"),
        P("head", "ctx"),
        P("ctx", "head"),
        P(),
    )
    out_specs = P(("ctx", "head"), None)
    return jax.shard_map(body, mesh=mesh, in_specs=in_specs, out_specs=out_specs, check_vma=False)
```

```python
import jax
import jax.numpy as jnp
from jax import lax
from jax.sharding import PartitionSpec as P

GROUP = 64


highest = lax.Precision.HIGHEST
norm_eps = 1e-06


def shifted(value, axis, steps):
    count = lax.axis_size(axis)
    first, last = (max(0, -steps), min(count, count - steps))
    return lax.ppermute(value, axis, [(source, source + steps) for source in range(first, last)])


def causal_conv(joined, taps, length):
    summed = jnp.zeros((length, joined.shape[1]), jnp.float32)
    for offset in range(taps.shape[0]):
        summed = summed + taps[offset] * joined[offset : offset + length].astype(jnp.float32)
    return jax.nn.silu(summed)


def unit_rows(matrix):
    return matrix * lax.rsqrt(jnp.sum(matrix * matrix, axis=-1, keepdims=True) + norm_eps)


def unit_lower_inverse(strict, row_ids, col_ids):
    length = strict.shape[-1]
    eye = (row_ids == col_ids).astype(jnp.float32)
    inverse = eye - jnp.where(row_ids // 2 == col_ids // 2, strict, 0.0)

    def level(depth, inverse):
        width = 2 << depth
        lower_left = jnp.where(
            (row_ids // (2 * width) == col_ids // (2 * width)) & (row_ids // width != col_ids // width),
            strict,
            0.0,
        )
        return inverse - matmul_pair(matmul_pair(inverse, lower_left), inverse)

    return lax.fori_loop(0, length.bit_length() - 2, level, inverse)


def group_terms(query, keys, values, beta, logdecay):
    length = logdecay.shape[-1]
    cumul = jnp.cumsum(logdecay, axis=-1)
    row_ids = lax.broadcasted_iota(jnp.int32, (length, length), 0)
    col_ids = lax.broadcasted_iota(jnp.int32, (length, length), 1)
    inside = col_ids <= row_ids
    differ = cumul[..., :, None] - cumul[..., None, :]
    decay_mask = jnp.where(inside, jnp.exp(jnp.where(inside, differ, 0.0)), 0.0)
    keygram = jnp.einsum("...ik,...jk->...ij", keys, keys, precision=highest)
    strict = jnp.where(col_ids < row_ids, beta[..., :, None] * keygram * decay_mask, 0.0)
    inverse = unit_lower_inverse(strict, row_ids, col_ids)
    upd_values = jnp.einsum(
        "...ij,...jd->...id", inverse, beta[..., None] * values, precision=highest
    )
    upd_keys = jnp.einsum(
        "...ij,...jd->...id", inverse, (beta * jnp.exp(cumul))[..., None] * keys, precision=highest
    )
    scores = jnp.einsum("...ik,...jk->...ij", query, keys, precision=highest) * decay_mask
    last_log = cumul[..., -1:]
    query_decay = query * jnp.exp(cumul)[..., None]
    key_decay = keys * jnp.exp(last_log - cumul)[..., None]
    return (upd_values, upd_keys, scores, query_decay, key_decay, last_log[..., 0])


def group_step(state, terms):
    upd_values, upd_keys, scores, query_decay, key_decay, last_log = terms
    new_values = upd_values - jnp.einsum("...ik,...kd->...id", upd_keys, state, precision=highest)
    output = jnp.einsum("...ik,...kd->...id", query_decay, state, precision=highest)
    output = output + jnp.einsum("...ij,...jd->...id", scores, new_values, precision=highest)
    state = jnp.exp(last_log)[..., None, None] * state + jnp.einsum(
        "...ik,...id->...kd", key_decay, new_values, precision=highest
    )
    return (state, output)


def matmul_pair(left_mats, right_mats):
    return jnp.einsum("...ij,...jk->...ik", left_mats, right_mats, precision=highest)


def body(
    query_in,
    key_in,
    value_in,
    query_taps,
    key_taps,
    value_taps,
    log_decay,
    beta_logit,
    gate_in,
    norm_gain,
):
    head_size = norm_gain.shape[0]
    length = query_in.shape[0]
    value_heads = log_decay.shape[0]
    key_heads = query_in.shape[1] // head_size
    share_ratio = value_heads // key_heads
    rim_width = query_taps.shape[0] - 1
    groups_dev = length // GROUP
    tail_rows = shifted(
        (
            query_in[length - rim_width :],
            key_in[length - rim_width :],
            value_in[length - rim_width :],
        ),
        "ctx",
        1,
    )
    query_conv = causal_conv(jnp.concatenate([tail_rows[0], query_in], axis=0), query_taps, length)
    key_conv = causal_conv(jnp.concatenate([tail_rows[1], key_in], axis=0), key_taps, length)
    value_conv = causal_conv(jnp.concatenate([tail_rows[2], value_in], axis=0), value_taps, length)
    queries = (
        unit_rows(query_conv.reshape(length, key_heads, head_size)) * head_size ** (-0.5)
    ).astype(jnp.bfloat16)
    keys = unit_rows(key_conv.reshape(length, key_heads, head_size)).astype(jnp.bfloat16)
    values = value_conv.reshape(length, value_heads, head_size).astype(jnp.bfloat16)

    def blocked(array):
        return (
            array.astype(jnp.float32)
            .reshape(groups_dev, GROUP, array.shape[1], head_size)
            .transpose(0, 2, 1, 3)
        )

    def blocked_rates(array):
        return array.reshape(value_heads, groups_dev, GROUP).transpose(1, 0, 2)

    query_blocks = blocked(jnp.repeat(queries, share_ratio, axis=1))
    key_blocks = blocked(jnp.repeat(keys, share_ratio, axis=1))
    value_blocks = blocked(values)
    beta_blocks = blocked_rates(jax.nn.sigmoid(beta_logit))
    decay_blocks = blocked_rates(log_decay)
    terms = group_terms(query_blocks, key_blocks, value_blocks, beta_blocks, decay_blocks)
    upd_values, upd_keys, scores, query_decay, key_decay, last_log = terms
    identity_state = jnp.broadcast_to(
        jnp.eye(head_size, dtype=jnp.float32), (value_heads, head_size, head_size)
    )
    group_maps = jnp.exp(last_log)[..., None, None] * identity_state - jnp.einsum(
        "...ik,...ij->...kj", key_decay, upd_keys, precision=highest
    )
    group_offsets = jnp.einsum("...ik,...id->...kd", key_decay, upd_values, precision=highest)
    query_effect = query_decay - matmul_pair(scores, upd_keys)
    zero_state = jnp.zeros((value_heads, head_size, head_size), jnp.float32)
    unit_span = jnp.concatenate([identity_state, zero_state], axis=-1)

    def compose(later, earlier):
        product = matmul_pair(later[..., :head_size], earlier)
        return product.at[..., head_size:].add(later[..., head_size:])

    group_ids = lax.broadcasted_iota(jnp.int32, (groups_dev, 1, 1, 1), 0)

    def group_round(depth, span):
        reach = 1 << depth
        prior = jnp.where(group_ids >= reach, jnp.roll(span, reach, axis=0), unit_span)
        return compose(span, prior)

    group_spans = lax.fori_loop(
        0,
        (groups_dev - 1).bit_length(),
        group_round,
        jnp.concatenate([group_maps, group_offsets], axis=-1),
    )
    entry_spans = jnp.where(group_ids >= 1, jnp.roll(group_spans, 1, axis=0), unit_span)
    entry_terms = matmul_pair(query_effect, entry_spans)
    state_effect = entry_terms[..., :head_size]
    local_out = entry_terms[..., head_size:] + matmul_pair(scores, upd_values)

    ctx_count = lax.axis_size("ctx")
    span = group_spans[-1]
    reach = 1
    while 2 * reach < ctx_count - 1:
        span = compose(span, shifted(span, "ctx", reach))
        reach *= 2
    pieces = -(-(ctx_count - 1) // reach)
    if pieces == 0:
        incoming = zero_state
    else:
        far = [shifted(span, "ctx", 1 + part * reach) for part in range(pieces - 1)]
        earliest = shifted(span[..., head_size:], "ctx", 1 + (pieces - 1) * reach)
        incoming = earliest
        for near in reversed(far):
            incoming = matmul_pair(near[..., :head_size], incoming) + near[..., head_size:]
    carried_out = jnp.einsum("ghik,hkd->ghid", state_effect, incoming, precision=highest)
    output = (local_out + carried_out).transpose(0, 2, 1, 3).reshape(length, value_heads, head_size)
    gates = gate_in.reshape(length, value_heads, head_size).astype(jnp.float32)
    normed = (
        output
        * lax.rsqrt(jnp.mean(output * output, axis=-1, keepdims=True) + norm_eps)
        * norm_gain
        * jax.nn.silu(gates)
    )
    normed = normed.astype(jnp.bfloat16).reshape(length, value_heads * head_size)
    return lax.all_to_all(normed, "head", split_axis=0, concat_axis=1, tiled=True)


def solution(mesh):
    in_specs = (
        P("ctx", "head"),
        P("ctx", "head"),
        P("ctx", "head"),
        P(None, "head"),
        P(None, "head"),
        P(None, "head"),
        P("head", "ctx"),
        P("head", "ctx"),
        P("ctx", "head"),
        P(),
    )
    out_specs = P(("ctx", "head"), None)
    return jax.shard_map(body, mesh=mesh, in_specs=in_specs, out_specs=out_specs, check_vma=False)
```

```python
import jax
import jax.numpy as jnp
from jax import lax
from jax.sharding import PartitionSpec as P

GROUP = 64


highest = lax.Precision.HIGHEST
norm_eps = 1e-06


def shifted(value, axis, steps):
    count = lax.axis_size(axis)
    first, last = (max(0, -steps), min(count, count - steps))
    return lax.ppermute(value, axis, [(source, source + steps) for source in range(first, last)])


def causal_conv(joined, taps, length):
    summed = jnp.zeros((length, joined.shape[1]), jnp.float32)
    for offset in range(taps.shape[0]):
        summed = summed + taps[offset] * joined[offset : offset + length].astype(jnp.float32)
    return jax.nn.silu(summed)


def unit_rows(matrix):
    return matrix * lax.rsqrt(jnp.sum(matrix * matrix, axis=-1, keepdims=True) + norm_eps)


def unit_lower_inverse(strict, row_ids, col_ids):
    length = strict.shape[-1]
    eye = (row_ids == col_ids).astype(jnp.float32)
    inverse = eye - jnp.where(row_ids // 2 == col_ids // 2, strict, 0.0)

    def level(depth, inverse):
        width = 2 << depth
        lower_left = jnp.where(
            (row_ids // (2 * width) == col_ids // (2 * width)) & (row_ids // width != col_ids // width),
            strict,
            0.0,
        )
        return inverse - matmul_pair(matmul_pair(inverse, lower_left), inverse)

    return lax.fori_loop(0, length.bit_length() - 2, level, inverse)


def group_terms(query, keys, values, beta, logdecay):
    length = logdecay.shape[-1]
    cumul = jnp.cumsum(logdecay, axis=-1)
    row_ids = lax.broadcasted_iota(jnp.int32, (length, length), 0)
    col_ids = lax.broadcasted_iota(jnp.int32, (length, length), 1)
    inside = col_ids <= row_ids
    differ = cumul[..., :, None] - cumul[..., None, :]
    decay_mask = jnp.where(inside, jnp.exp(jnp.where(inside, differ, 0.0)), 0.0)
    keygram = jnp.einsum("...ik,...jk->...ij", keys, keys, precision=highest)
    strict = jnp.where(col_ids < row_ids, beta[..., :, None] * keygram * decay_mask, 0.0)
    inverse = unit_lower_inverse(strict, row_ids, col_ids)
    upd_values = jnp.einsum(
        "...ij,...jd->...id", inverse, beta[..., None] * values, precision=highest
    )
    upd_keys = jnp.einsum(
        "...ij,...jd->...id", inverse, (beta * jnp.exp(cumul))[..., None] * keys, precision=highest
    )
    scores = jnp.einsum("...ik,...jk->...ij", query, keys, precision=highest) * decay_mask
    last_log = cumul[..., -1:]
    query_decay = query * jnp.exp(cumul)[..., None]
    key_decay = keys * jnp.exp(last_log - cumul)[..., None]
    return (upd_values, upd_keys, scores, query_decay, key_decay, last_log[..., 0])


def group_step(state, terms):
    upd_values, upd_keys, scores, query_decay, key_decay, last_log = terms
    new_values = upd_values - jnp.einsum("...ik,...kd->...id", upd_keys, state, precision=highest)
    output = jnp.einsum("...ik,...kd->...id", query_decay, state, precision=highest)
    output = output + jnp.einsum("...ij,...jd->...id", scores, new_values, precision=highest)
    state = jnp.exp(last_log)[..., None, None] * state + jnp.einsum(
        "...ik,...id->...kd", key_decay, new_values, precision=highest
    )
    return (state, output)


def matmul_pair(left_mats, right_mats):
    return jnp.einsum("...ij,...jk->...ik", left_mats, right_mats, precision=highest)


def body(
    query_in,
    key_in,
    value_in,
    query_taps,
    key_taps,
    value_taps,
    log_decay,
    beta_logit,
    gate_in,
    norm_gain,
):
    head_size = norm_gain.shape[0]
    length = query_in.shape[0]
    value_heads = log_decay.shape[0]
    key_heads = query_in.shape[1] // head_size
    share_ratio = value_heads // key_heads
    rim_width = query_taps.shape[0] - 1
    groups_dev = length // GROUP
    tail_rows = shifted(
        (
            query_in[length - rim_width :],
            key_in[length - rim_width :],
            value_in[length - rim_width :],
        ),
        "ctx",
        1,
    )
    query_conv = causal_conv(jnp.concatenate([tail_rows[0], query_in], axis=0), query_taps, length)
    key_conv = causal_conv(jnp.concatenate([tail_rows[1], key_in], axis=0), key_taps, length)
    value_conv = causal_conv(jnp.concatenate([tail_rows[2], value_in], axis=0), value_taps, length)
    queries = (
        unit_rows(query_conv.reshape(length, key_heads, head_size)) * head_size ** (-0.5)
    ).astype(jnp.bfloat16)
    keys = unit_rows(key_conv.reshape(length, key_heads, head_size)).astype(jnp.bfloat16)
    values = value_conv.reshape(length, value_heads, head_size).astype(jnp.bfloat16)

    def blocked(array):
        return (
            array.astype(jnp.float32)
            .reshape(groups_dev, GROUP, array.shape[1], head_size)
            .transpose(0, 2, 1, 3)
        )

    def blocked_rates(array):
        return array.reshape(value_heads, groups_dev, GROUP).transpose(1, 0, 2)

    query_blocks = blocked(jnp.repeat(queries, share_ratio, axis=1))
    key_blocks = blocked(jnp.repeat(keys, share_ratio, axis=1))
    value_blocks = blocked(values)
    beta_blocks = blocked_rates(jax.nn.sigmoid(beta_logit))
    decay_blocks = blocked_rates(log_decay)
    terms = group_terms(query_blocks, key_blocks, value_blocks, beta_blocks, decay_blocks)
    upd_values, upd_keys, scores, query_decay, key_decay, last_log = terms
    identity_state = jnp.broadcast_to(
        jnp.eye(head_size, dtype=jnp.float32), (value_heads, head_size, head_size)
    )
    group_maps = jnp.exp(last_log)[..., None, None] * identity_state - jnp.einsum(
        "...ik,...ij->...kj", key_decay, upd_keys, precision=highest
    )
    group_offsets = jnp.einsum("...ik,...id->...kd", key_decay, upd_values, precision=highest)
    query_effect = query_decay - matmul_pair(scores, upd_keys)
    zero_state = jnp.zeros((value_heads, head_size, head_size), jnp.float32)

    span_maps, span_offsets = group_maps, group_offsets
    reach = 1
    while reach < groups_dev:
        prior_maps = jnp.concatenate(
            [jnp.broadcast_to(identity_state, (reach,) + identity_state.shape), span_maps[: groups_dev - reach]]
        )
        prior_offsets = jnp.concatenate(
            [jnp.broadcast_to(zero_state, (reach,) + zero_state.shape), span_offsets[: groups_dev - reach]]
        )
        span_offsets = matmul_pair(span_maps, prior_offsets) + span_offsets
        span_maps = matmul_pair(span_maps, prior_maps)
        reach *= 2
    shard_map_mat, local_state = span_maps[-1], span_offsets[-1]
    entry_maps = jnp.concatenate([identity_state[None], span_maps[:-1]])
    entry_offsets = jnp.concatenate([zero_state[None], span_offsets[:-1]])
    state_effect = matmul_pair(query_effect, entry_maps)
    local_out = matmul_pair(query_effect, entry_offsets) + matmul_pair(scores, upd_values)

    ctx_count = lax.axis_size("ctx")
    span_map, span_state = shard_map_mat, local_state
    reach = 1
    while 2 * reach < ctx_count - 1:
        prior_map, prior_state = shifted((span_map, span_state), "ctx", reach)
        span_state = matmul_pair(span_map, prior_state) + span_state
        span_map = matmul_pair(span_map, prior_map)
        reach *= 2
    pieces = -(-(ctx_count - 1) // reach)
    if pieces == 0:
        incoming = zero_state
    else:
        far = [shifted((span_map, span_state), "ctx", 1 + part * reach) for part in range(pieces - 1)]
        incoming = shifted(span_state, "ctx", 1 + (pieces - 1) * reach)
        for near_map, near_state in reversed(far):
            incoming = matmul_pair(near_map, incoming) + near_state
    carried_out = jnp.einsum("ghik,hkd->ghid", state_effect, incoming, precision=highest)
    output = (local_out + carried_out).transpose(0, 2, 1, 3).reshape(length, value_heads, head_size)
    gates = gate_in.reshape(length, value_heads, head_size).astype(jnp.float32)
    normed = (
        output
        * lax.rsqrt(jnp.mean(output * output, axis=-1, keepdims=True) + norm_eps)
        * norm_gain
        * jax.nn.silu(gates)
    )
    normed = normed.astype(jnp.bfloat16).reshape(length, value_heads * head_size)
    return lax.all_to_all(normed, "head", split_axis=0, concat_axis=1, tiled=True)


def solution(mesh):
    in_specs = (
        P("ctx", "head"),
        P("ctx", "head"),
        P("ctx", "head"),
        P(None, "head"),
        P(None, "head"),
        P(None, "head"),
        P("head", "ctx"),
        P("head", "ctx"),
        P("ctx", "head"),
        P(),
    )
    out_specs = P(("ctx", "head"), None)
    return jax.shard_map(body, mesh=mesh, in_specs=in_specs, out_specs=out_specs, check_vma=False)
```

```python
import jax
import jax.numpy as jnp
from jax import lax
from jax.sharding import PartitionSpec as P

GROUP = 64


highest = lax.Precision.HIGHEST
norm_eps = 1e-06


def shifted(value, axis, steps):
    count = lax.axis_size(axis)
    first, last = (max(0, -steps), min(count, count - steps))
    return lax.ppermute(value, axis, [(source, source + steps) for source in range(first, last)])


def causal_conv(joined, taps, length):
    summed = jnp.zeros((length, joined.shape[1]), jnp.float32)
    for offset in range(taps.shape[0]):
        summed = summed + taps[offset] * joined[offset : offset + length].astype(jnp.float32)
    return jax.nn.silu(summed)


def unit_rows(matrix):
    return matrix * lax.rsqrt(jnp.sum(matrix * matrix, axis=-1, keepdims=True) + norm_eps)


def unit_lower_inverse(strict, row_ids, col_ids):
    length = strict.shape[-1]
    eye = (row_ids == col_ids).astype(jnp.float32)
    inverse = eye - jnp.where(row_ids // 2 == col_ids // 2, strict, 0.0)

    def level(depth, inverse):
        width = 2 << depth
        lower_left = jnp.where(
            (row_ids // (2 * width) == col_ids // (2 * width)) & (row_ids // width != col_ids // width),
            strict,
            0.0,
        )
        return inverse - matmul_pair(matmul_pair(inverse, lower_left), inverse)

    return lax.fori_loop(0, length.bit_length() - 2, level, inverse)


def group_terms(query, keys, values, beta, logdecay):
    length = logdecay.shape[-1]
    cumul = jnp.cumsum(logdecay, axis=-1)
    row_ids = lax.broadcasted_iota(jnp.int32, (length, length), 0)
    col_ids = lax.broadcasted_iota(jnp.int32, (length, length), 1)
    inside = col_ids <= row_ids
    differ = cumul[..., :, None] - cumul[..., None, :]
    decay_mask = jnp.where(inside, jnp.exp(jnp.where(inside, differ, 0.0)), 0.0)
    grams = jnp.einsum(
        "...ik,...jk->...ij", jnp.concatenate([keys, query], axis=-2), keys, precision=highest
    )
    keygram = grams[..., :length, :]
    strict = jnp.where(col_ids < row_ids, beta[..., :, None] * keygram * decay_mask, 0.0)
    inverse = unit_lower_inverse(strict, row_ids, col_ids)
    updates = jnp.einsum(
        "...ij,...jd->...id",
        inverse,
        jnp.concatenate([beta[..., None] * values, (beta * jnp.exp(cumul))[..., None] * keys], axis=-1),
        precision=highest,
    )
    upd_values = updates[..., : values.shape[-1]]
    upd_keys = updates[..., values.shape[-1] :]
    scores = grams[..., length:, :] * decay_mask
    last_log = cumul[..., -1:]
    query_decay = query * jnp.exp(cumul)[..., None]
    key_decay = keys * jnp.exp(last_log - cumul)[..., None]
    return (upd_values, upd_keys, scores, query_decay, key_decay, last_log[..., 0])


def group_step(state, terms):
    upd_values, upd_keys, scores, query_decay, key_decay, last_log = terms
    new_values = upd_values - jnp.einsum("...ik,...kd->...id", upd_keys, state, precision=highest)
    output = jnp.einsum("...ik,...kd->...id", query_decay, state, precision=highest)
    output = output + jnp.einsum("...ij,...jd->...id", scores, new_values, precision=highest)
    state = jnp.exp(last_log)[..., None, None] * state + jnp.einsum(
        "...ik,...id->...kd", key_decay, new_values, precision=highest
    )
    return (state, output)


def matmul_pair(left_mats, right_mats):
    return jnp.einsum("...ij,...jk->...ik", left_mats, right_mats, precision=highest)


def body(
    query_in,
    key_in,
    value_in,
    query_taps,
    key_taps,
    value_taps,
    log_decay,
    beta_logit,
    gate_in,
    norm_gain,
):
    head_size = norm_gain.shape[0]
    length = query_in.shape[0]
    value_heads = log_decay.shape[0]
    key_heads = query_in.shape[1] // head_size
    share_ratio = value_heads // key_heads
    rim_width = query_taps.shape[0] - 1
    groups_dev = length // GROUP
    query_width, key_width = query_in.shape[1], key_in.shape[1]
    tails = shifted(
        jnp.concatenate(
            [query_in[length - rim_width :], key_in[length - rim_width :], value_in[length - rim_width :]],
            axis=1,
        ),
        "ctx",
        1,
    )
    tail_rows = (
        tails[:, :query_width],
        tails[:, query_width : query_width + key_width],
        tails[:, query_width + key_width :],
    )
    query_conv = causal_conv(jnp.concatenate([tail_rows[0], query_in], axis=0), query_taps, length)
    key_conv = causal_conv(jnp.concatenate([tail_rows[1], key_in], axis=0), key_taps, length)
    value_conv = causal_conv(jnp.concatenate([tail_rows[2], value_in], axis=0), value_taps, length)
    queries = (
        unit_rows(query_conv.reshape(length, key_heads, head_size)) * head_size ** (-0.5)
    ).astype(jnp.bfloat16)
    keys = unit_rows(key_conv.reshape(length, key_heads, head_size)).astype(jnp.bfloat16)
    values = value_conv.reshape(length, value_heads, head_size).astype(jnp.bfloat16)

    def blocked(array):
        return (
            array.astype(jnp.float32)
            .reshape(groups_dev, GROUP, array.shape[1], head_size)
            .transpose(0, 2, 1, 3)
        )

    def blocked_rates(array):
        return array.reshape(value_heads, groups_dev, GROUP).transpose(1, 0, 2)

    query_blocks = blocked(jnp.repeat(queries, share_ratio, axis=1))
    key_blocks = blocked(jnp.repeat(keys, share_ratio, axis=1))
    value_blocks = blocked(values)
    beta_blocks = blocked_rates(jax.nn.sigmoid(beta_logit))
    decay_blocks = blocked_rates(log_decay)
    terms = group_terms(query_blocks, key_blocks, value_blocks, beta_blocks, decay_blocks)
    upd_values, upd_keys, scores, query_decay, key_decay, last_log = terms
    identity_state = jnp.broadcast_to(
        jnp.eye(head_size, dtype=jnp.float32), (value_heads, head_size, head_size)
    )
    map_terms = jnp.einsum(
        "...ik,...ij->...kj", key_decay, jnp.concatenate([upd_keys, upd_values], axis=-1), precision=highest
    )
    group_maps = jnp.exp(last_log)[..., None, None] * identity_state - map_terms[..., :head_size]
    group_offsets = map_terms[..., head_size:]
    score_terms = matmul_pair(scores, jnp.concatenate([upd_keys, upd_values], axis=-1))
    query_effect = query_decay - score_terms[..., :head_size]
    zero_state = jnp.zeros((value_heads, head_size, head_size), jnp.float32)
    unit_span = jnp.concatenate([identity_state, zero_state], axis=-1)

    def compose(later, earlier):
        product = matmul_pair(later[..., :head_size], earlier)
        return product + jnp.concatenate([jnp.zeros_like(later[..., :head_size]), later[..., head_size:]], axis=-1)

    spans = jnp.concatenate([group_maps, group_offsets], axis=-1)
    reach = 1
    while reach < groups_dev:
        prior = jnp.concatenate(
            [jnp.broadcast_to(unit_span, (reach,) + unit_span.shape), spans[: groups_dev - reach]]
        )
        spans = compose(spans, prior)
        reach *= 2
    shard_map_mat, local_state = spans[-1][..., :head_size], spans[-1][..., head_size:]
    entry_terms = matmul_pair(query_effect, jnp.concatenate([unit_span[None], spans[:-1]]))
    state_effect = entry_terms[..., :head_size]
    local_out = entry_terms[..., head_size:] + score_terms[..., head_size:]

    ctx_count = lax.axis_size("ctx")
    span_map, span_state = shard_map_mat, local_state
    reach = 1
    while reach < ctx_count:
        if 2 * reach < ctx_count:
            prior_map, prior_state = shifted((span_map, span_state), "ctx", reach)
            span_state = matmul_pair(span_map, prior_state) + span_state
            span_map = matmul_pair(span_map, prior_map)
        else:
            prior_state = shifted(span_state, "ctx", reach)
            span_state = matmul_pair(span_map, prior_state) + span_state
        reach *= 2
    incoming = shifted(span_state, "ctx", 1)

    carried_out = jnp.einsum("ghik,hkd->ghid", state_effect, incoming, precision=highest)
    output = (local_out + carried_out).transpose(0, 2, 1, 3).reshape(length, value_heads, head_size)
    gates = gate_in.reshape(length, value_heads, head_size).astype(jnp.float32)
    normed = (
        output
        * lax.rsqrt(jnp.mean(output * output, axis=-1, keepdims=True) + norm_eps)
        * norm_gain
        * jax.nn.silu(gates)
    )
    normed = normed.astype(jnp.bfloat16).reshape(length, value_heads * head_size)
    return lax.all_to_all(normed, "head", split_axis=0, concat_axis=1, tiled=True)


def solution(mesh):
    in_specs = (
        P("ctx", "head"),
        P("ctx", "head"),
        P("ctx", "head"),
        P(None, "head"),
        P(None, "head"),
        P(None, "head"),
        P("head", "ctx"),
        P("head", "ctx"),
        P("ctx", "head"),
        P(),
    )
    out_specs = P(("ctx", "head"), None)
    return jax.shard_map(body, mesh=mesh, in_specs=in_specs, out_specs=out_specs, check_vma=False)
```

```python
import jax
import jax.numpy as jnp
from jax import lax
from jax.sharding import PartitionSpec as P

GROUP = 64


highest = lax.Precision.HIGHEST
high = lax.Precision.HIGH
norm_eps = 1e-06


def shifted(value, axis, steps):
    count = lax.axis_size(axis)
    first, last = (max(0, -steps), min(count, count - steps))
    return lax.ppermute(value, axis, [(source, source + steps) for source in range(first, last)])


def causal_conv(joined, taps, length):
    summed = jnp.zeros((length, joined.shape[1]), jnp.float32)
    for offset in range(taps.shape[0]):
        summed = summed + taps[offset] * joined[offset : offset + length].astype(jnp.float32)
    return jax.nn.silu(summed)


def unit_rows(matrix):
    return matrix * lax.rsqrt(jnp.sum(matrix * matrix, axis=-1, keepdims=True) + norm_eps)


def unit_lower_inverse(strict, row_ids, col_ids):
    length = strict.shape[-1]
    eye = (row_ids == col_ids).astype(jnp.float32)
    inverse = eye - jnp.where(row_ids // 2 == col_ids // 2, strict, 0.0)

    def level(depth, inverse):
        width = 2 << depth
        lower_left = jnp.where(
            (row_ids // (2 * width) == col_ids // (2 * width)) & (row_ids // width != col_ids // width),
            strict,
            0.0,
        )
        return inverse - matmul_pair(matmul_pair(inverse, lower_left, highest), inverse, highest)

    return lax.fori_loop(0, length.bit_length() - 2, level, inverse)


def group_terms(query, keys, values, beta, logdecay):
    length = logdecay.shape[-1]
    cumul = jnp.cumsum(logdecay, axis=-1)
    row_ids = lax.broadcasted_iota(jnp.int32, (length, length), 0)
    col_ids = lax.broadcasted_iota(jnp.int32, (length, length), 1)
    inside = col_ids <= row_ids
    differ = cumul[..., :, None] - cumul[..., None, :]
    decay_mask = jnp.where(inside, jnp.exp(jnp.where(inside, differ, 0.0)), 0.0)
    grams = jnp.einsum(
        "...ik,...jk->...ij", jnp.concatenate([keys, query], axis=-2), keys, precision=highest
    )
    keygram = grams[..., :length, :]
    strict = jnp.where(col_ids < row_ids, beta[..., :, None] * keygram * decay_mask, 0.0)
    inverse = unit_lower_inverse(strict, row_ids, col_ids)
    updates = jnp.einsum(
        "...ij,...jd->...id",
        inverse,
        jnp.concatenate([beta[..., None] * values, (beta * jnp.exp(cumul))[..., None] * keys], axis=-1),
        precision=high,
    )
    upd_values = updates[..., : values.shape[-1]]
    upd_keys = updates[..., values.shape[-1] :]
    scores = grams[..., length:, :] * decay_mask
    last_log = cumul[..., -1:]
    query_decay = query * jnp.exp(cumul)[..., None]
    key_decay = keys * jnp.exp(last_log - cumul)[..., None]
    return (upd_values, upd_keys, scores, query_decay, key_decay, last_log[..., 0])


def group_step(state, terms):
    upd_values, upd_keys, scores, query_decay, key_decay, last_log = terms
    new_values = upd_values - jnp.einsum("...ik,...kd->...id", upd_keys, state, precision=highest)
    output = jnp.einsum("...ik,...kd->...id", query_decay, state, precision=highest)
    output = output + jnp.einsum("...ij,...jd->...id", scores, new_values, precision=highest)
    state = jnp.exp(last_log)[..., None, None] * state + jnp.einsum(
        "...ik,...id->...kd", key_decay, new_values, precision=highest
    )
    return (state, output)


def matmul_pair(left_mats, right_mats, precision=high):
    return jnp.einsum("...ij,...jk->...ik", left_mats, right_mats, precision=precision)


def body(
    query_in,
    key_in,
    value_in,
    query_taps,
    key_taps,
    value_taps,
    log_decay,
    beta_logit,
    gate_in,
    norm_gain,
):
    head_size = norm_gain.shape[0]
    length = query_in.shape[0]
    value_heads = log_decay.shape[0]
    key_heads = query_in.shape[1] // head_size
    share_ratio = value_heads // key_heads
    rim_width = query_taps.shape[0] - 1
    groups_dev = length // GROUP
    query_width, key_width = query_in.shape[1], key_in.shape[1]
    tails = shifted(
        jnp.concatenate(
            [query_in[length - rim_width :], key_in[length - rim_width :], value_in[length - rim_width :]],
            axis=1,
        ),
        "ctx",
        1,
    )
    tail_rows = (
        tails[:, :query_width],
        tails[:, query_width : query_width + key_width],
        tails[:, query_width + key_width :],
    )
    query_conv = causal_conv(jnp.concatenate([tail_rows[0], query_in], axis=0), query_taps, length)
    key_conv = causal_conv(jnp.concatenate([tail_rows[1], key_in], axis=0), key_taps, length)
    value_conv = causal_conv(jnp.concatenate([tail_rows[2], value_in], axis=0), value_taps, length)
    queries = (
        unit_rows(query_conv.reshape(length, key_heads, head_size)) * head_size ** (-0.5)
    ).astype(jnp.bfloat16)
    keys = unit_rows(key_conv.reshape(length, key_heads, head_size)).astype(jnp.bfloat16)
    values = value_conv.reshape(length, value_heads, head_size).astype(jnp.bfloat16)

    def blocked(array):
        return (
            array.astype(jnp.float32)
            .reshape(groups_dev, GROUP, array.shape[1], head_size)
            .transpose(0, 2, 1, 3)
        )

    def blocked_rates(array):
        return array.reshape(value_heads, groups_dev, GROUP).transpose(1, 0, 2)

    query_blocks = blocked(jnp.repeat(queries, share_ratio, axis=1))
    key_blocks = blocked(jnp.repeat(keys, share_ratio, axis=1))
    value_blocks = blocked(values)
    beta_blocks = blocked_rates(jax.nn.sigmoid(beta_logit))
    decay_blocks = blocked_rates(log_decay)
    terms = group_terms(query_blocks, key_blocks, value_blocks, beta_blocks, decay_blocks)
    upd_values, upd_keys, scores, query_decay, key_decay, last_log = terms
    identity_state = jnp.broadcast_to(
        jnp.eye(head_size, dtype=jnp.float32), (value_heads, head_size, head_size)
    )
    map_terms = jnp.einsum(
        "...ik,...ij->...kj", key_decay, jnp.concatenate([upd_keys, upd_values], axis=-1), precision=high
    )
    group_maps = jnp.exp(last_log)[..., None, None] * identity_state - map_terms[..., :head_size]
    group_offsets = map_terms[..., head_size:]
    score_terms = matmul_pair(scores, jnp.concatenate([upd_keys, upd_values], axis=-1))
    query_effect = query_decay - score_terms[..., :head_size]
    zero_state = jnp.zeros((value_heads, head_size, head_size), jnp.float32)
    unit_span = jnp.concatenate([identity_state, zero_state], axis=-1)

    def compose(later, earlier):
        product = matmul_pair(later[..., :head_size], earlier)
        return product + jnp.concatenate([jnp.zeros_like(later[..., :head_size]), later[..., head_size:]], axis=-1)

    spans = jnp.concatenate([group_maps, group_offsets], axis=-1)
    reach = 1
    while reach < groups_dev:
        prior = jnp.concatenate(
            [jnp.broadcast_to(unit_span, (reach,) + unit_span.shape), spans[: groups_dev - reach]]
        )
        spans = compose(spans, prior)
        reach *= 2
    shard_map_mat, local_state = spans[-1][..., :head_size], spans[-1][..., head_size:]
    entry_terms = matmul_pair(query_effect, jnp.concatenate([unit_span[None], spans[:-1]]))
    state_effect = entry_terms[..., :head_size]
    local_out = entry_terms[..., head_size:] + score_terms[..., head_size:]

    ctx_count = lax.axis_size("ctx")
    span_map, span_state = shard_map_mat, local_state
    reach = 1
    while reach < ctx_count:
        if 2 * reach < ctx_count:
            prior_map, prior_state = shifted((span_map, span_state), "ctx", reach)
            span_state = matmul_pair(span_map, prior_state) + span_state
            span_map = matmul_pair(span_map, prior_map)
        else:
            prior_state = shifted(span_state, "ctx", reach)
            span_state = matmul_pair(span_map, prior_state) + span_state
        reach *= 2
    incoming = shifted(span_state, "ctx", 1)

    carried_out = jnp.einsum("ghik,hkd->ghid", state_effect, incoming, precision=high)
    output = (local_out + carried_out).transpose(0, 2, 1, 3).reshape(length, value_heads, head_size)
    gates = gate_in.reshape(length, value_heads, head_size).astype(jnp.float32)
    normed = (
        output
        * lax.rsqrt(jnp.mean(output * output, axis=-1, keepdims=True) + norm_eps)
        * norm_gain
        * jax.nn.silu(gates)
    )
    normed = normed.astype(jnp.bfloat16).reshape(length, value_heads * head_size)
    return lax.all_to_all(normed, "head", split_axis=0, concat_axis=1, tiled=True)


def solution(mesh):
    in_specs = (
        P("ctx", "head"),
        P("ctx", "head"),
        P("ctx", "head"),
        P(None, "head"),
        P(None, "head"),
        P(None, "head"),
        P("head", "ctx"),
        P("head", "ctx"),
        P("ctx", "head"),
        P(),
    )
    out_specs = P(("ctx", "head"), None)
    return jax.shard_map(body, mesh=mesh, in_specs=in_specs, out_specs=out_specs, check_vma=False)
```

```python
import jax
import jax.numpy as jnp
from jax import lax
from jax.sharding import PartitionSpec as P

GROUP = 64


highest = lax.Precision.HIGHEST
high = lax.Precision.HIGH
norm_eps = 1e-06


def shifted(value, axis, steps):
    count = lax.axis_size(axis)
    first, last = (max(0, -steps), min(count, count - steps))
    return lax.ppermute(value, axis, [(source, source + steps) for source in range(first, last)])


def shifted_split(value, axis, steps):
    halves = [(part[: part.shape[0] // 2], part[part.shape[0] // 2 :]) for part in value]
    moved = shifted(halves, axis, steps)
    return tuple(jnp.concatenate(pair, axis=0) for pair in moved)


def causal_conv(joined, taps, length):
    summed = jnp.zeros((length, joined.shape[1]), jnp.float32)
    for offset in range(taps.shape[0]):
        summed = summed + taps[offset] * joined[offset : offset + length].astype(jnp.float32)
    return jax.nn.silu(summed)


def unit_rows(matrix):
    return matrix * lax.rsqrt(jnp.sum(matrix * matrix, axis=-1, keepdims=True) + norm_eps)


def unit_lower_inverse(strict, row_ids, col_ids):
    length = strict.shape[-1]
    eye = (row_ids == col_ids).astype(jnp.float32)
    inverse = eye - jnp.where(row_ids // 2 == col_ids // 2, strict, 0.0)

    def level(depth, inverse):
        width = 2 << depth
        lower_left = jnp.where(
            (row_ids // (2 * width) == col_ids // (2 * width)) & (row_ids // width != col_ids // width),
            strict,
            0.0,
        )
        return inverse - matmul_pair(matmul_pair(inverse, lower_left, highest), inverse, highest)

    return lax.fori_loop(0, length.bit_length() - 2, level, inverse)


def group_terms(query, keys, values, beta, logdecay):
    length = logdecay.shape[-1]
    cumul = jnp.cumsum(logdecay, axis=-1)
    row_ids = lax.broadcasted_iota(jnp.int32, (length, length), 0)
    col_ids = lax.broadcasted_iota(jnp.int32, (length, length), 1)
    inside = col_ids <= row_ids
    differ = cumul[..., :, None] - cumul[..., None, :]
    decay_mask = jnp.where(inside, jnp.exp(jnp.where(inside, differ, 0.0)), 0.0)
    grams = jnp.einsum(
        "...ik,...jk->...ij", jnp.concatenate([keys, query], axis=-2), keys, precision=highest
    )
    keygram = grams[..., :length, :]
    strict = jnp.where(col_ids < row_ids, beta[..., :, None] * keygram * decay_mask, 0.0)
    inverse = unit_lower_inverse(strict, row_ids, col_ids)
    updates = jnp.einsum(
        "...ij,...jd->...id",
        inverse,
        jnp.concatenate([beta[..., None] * values, (beta * jnp.exp(cumul))[..., None] * keys], axis=-1),
        precision=high,
    )
    upd_values = updates[..., : values.shape[-1]]
    upd_keys = updates[..., values.shape[-1] :]
    scores = grams[..., length:, :] * decay_mask
    last_log = cumul[..., -1:]
    query_decay = query * jnp.exp(cumul)[..., None]
    key_decay = keys * jnp.exp(last_log - cumul)[..., None]
    return (upd_values, upd_keys, scores, query_decay, key_decay, last_log[..., 0])


def group_step(state, terms):
    upd_values, upd_keys, scores, query_decay, key_decay, last_log = terms
    new_values = upd_values - jnp.einsum("...ik,...kd->...id", upd_keys, state, precision=highest)
    output = jnp.einsum("...ik,...kd->...id", query_decay, state, precision=highest)
    output = output + jnp.einsum("...ij,...jd->...id", scores, new_values, precision=highest)
    state = jnp.exp(last_log)[..., None, None] * state + jnp.einsum(
        "...ik,...id->...kd", key_decay, new_values, precision=highest
    )
    return (state, output)


def matmul_pair(left_mats, right_mats, precision=high):
    return jnp.einsum("...ij,...jk->...ik", left_mats, right_mats, precision=precision)


def body(
    query_in,
    key_in,
    value_in,
    query_taps,
    key_taps,
    value_taps,
    log_decay,
    beta_logit,
    gate_in,
    norm_gain,
):
    head_size = norm_gain.shape[0]
    length = query_in.shape[0]
    value_heads = log_decay.shape[0]
    key_heads = query_in.shape[1] // head_size
    share_ratio = value_heads // key_heads
    rim_width = query_taps.shape[0] - 1
    groups_dev = length // GROUP
    query_width, key_width = query_in.shape[1], key_in.shape[1]
    tails = shifted(
        jnp.concatenate(
            [query_in[length - rim_width :], key_in[length - rim_width :], value_in[length - rim_width :]],
            axis=1,
        ),
        "ctx",
        1,
    )
    tail_rows = (
        tails[:, :query_width],
        tails[:, query_width : query_width + key_width],
        tails[:, query_width + key_width :],
    )
    query_conv = causal_conv(jnp.concatenate([tail_rows[0], query_in], axis=0), query_taps, length)
    key_conv = causal_conv(jnp.concatenate([tail_rows[1], key_in], axis=0), key_taps, length)
    value_conv = causal_conv(jnp.concatenate([tail_rows[2], value_in], axis=0), value_taps, length)
    queries = (
        unit_rows(query_conv.reshape(length, key_heads, head_size)) * head_size ** (-0.5)
    ).astype(jnp.bfloat16)
    keys = unit_rows(key_conv.reshape(length, key_heads, head_size)).astype(jnp.bfloat16)
    values = value_conv.reshape(length, value_heads, head_size).astype(jnp.bfloat16)

    def blocked(array):
        return (
            array.astype(jnp.float32)
            .reshape(groups_dev, GROUP, array.shape[1], head_size)
            .transpose(0, 2, 1, 3)
        )

    def blocked_rates(array):
        return array.reshape(value_heads, groups_dev, GROUP).transpose(1, 0, 2)

    query_blocks = blocked(jnp.repeat(queries, share_ratio, axis=1))
    key_blocks = blocked(jnp.repeat(keys, share_ratio, axis=1))
    value_blocks = blocked(values)
    beta_blocks = blocked_rates(jax.nn.sigmoid(beta_logit))
    decay_blocks = blocked_rates(log_decay)
    terms = group_terms(query_blocks, key_blocks, value_blocks, beta_blocks, decay_blocks)
    upd_values, upd_keys, scores, query_decay, key_decay, last_log = terms
    identity_state = jnp.broadcast_to(
        jnp.eye(head_size, dtype=jnp.float32), (value_heads, head_size, head_size)
    )
    map_terms = jnp.einsum(
        "...ik,...ij->...kj", key_decay, jnp.concatenate([upd_keys, upd_values], axis=-1), precision=high
    )
    group_maps = jnp.exp(last_log)[..., None, None] * identity_state - map_terms[..., :head_size]
    group_offsets = map_terms[..., head_size:]
    score_terms = matmul_pair(scores, jnp.concatenate([upd_keys, upd_values], axis=-1))
    query_effect = query_decay - score_terms[..., :head_size]
    zero_state = jnp.zeros((value_heads, head_size, head_size), jnp.float32)
    unit_span = jnp.concatenate([identity_state, zero_state], axis=-1)

    def compose(later, earlier):
        product = matmul_pair(later[..., :head_size], earlier)
        return product + jnp.concatenate([jnp.zeros_like(later[..., :head_size]), later[..., head_size:]], axis=-1)

    spans = jnp.concatenate([group_maps, group_offsets], axis=-1)
    reach = 1
    while reach < groups_dev:
        prior = jnp.concatenate(
            [jnp.broadcast_to(unit_span, (reach,) + unit_span.shape), spans[: groups_dev - reach]]
        )
        spans = compose(spans, prior)
        reach *= 2
    shard_map_mat, local_state = spans[-1][..., :head_size], spans[-1][..., head_size:]
    entry_terms = matmul_pair(query_effect, jnp.concatenate([unit_span[None], spans[:-1]]))
    state_effect = entry_terms[..., :head_size]
    local_out = entry_terms[..., head_size:] + score_terms[..., head_size:]

    ctx_count = lax.axis_size("ctx")
    span_map, span_state = shard_map_mat, local_state
    reach = 1
    while reach < ctx_count:
        if 2 * reach < ctx_count:
            prior_map, prior_state = shifted_split((span_map, span_state), "ctx", reach)
            span_state = matmul_pair(span_map, prior_state) + span_state
            span_map = matmul_pair(span_map, prior_map)
        else:
            (prior_state,) = shifted_split((span_state,), "ctx", reach)
            span_state = matmul_pair(span_map, prior_state) + span_state
        reach *= 2
    (incoming,) = shifted_split((span_state,), "ctx", 1)

    carried_out = jnp.einsum("ghik,hkd->ghid", state_effect, incoming, precision=high)
    output = (local_out + carried_out).transpose(0, 2, 1, 3).reshape(length, value_heads, head_size)
    gates = gate_in.reshape(length, value_heads, head_size).astype(jnp.float32)
    normed = (
        output
        * lax.rsqrt(jnp.mean(output * output, axis=-1, keepdims=True) + norm_eps)
        * norm_gain
        * jax.nn.silu(gates)
    )
    normed = normed.astype(jnp.bfloat16).reshape(length, value_heads * head_size)
    return lax.all_to_all(normed, "head", split_axis=0, concat_axis=1, tiled=True)


def solution(mesh):
    in_specs = (
        P("ctx", "head"),
        P("ctx", "head"),
        P("ctx", "head"),
        P(None, "head"),
        P(None, "head"),
        P(None, "head"),
        P("head", "ctx"),
        P("head", "ctx"),
        P("ctx", "head"),
        P(),
    )
    out_specs = P(("ctx", "head"), None)
    return jax.shard_map(body, mesh=mesh, in_specs=in_specs, out_specs=out_specs, check_vma=False)
```

```python
import jax
import jax.numpy as jnp
from jax import lax
from jax.sharding import PartitionSpec as P

GROUP = 64


highest = lax.Precision.HIGHEST
high = lax.Precision.HIGH
norm_eps = 1e-06


def shifted(value, axis, steps):
    count = lax.axis_size(axis)
    first, last = (max(0, -steps), min(count, count - steps))
    return lax.ppermute(value, axis, [(source, source + steps) for source in range(first, last)])


def causal_conv(joined, taps, length):
    summed = jnp.zeros((length, joined.shape[1]), jnp.float32)
    for offset in range(taps.shape[0]):
        summed = summed + taps[offset] * joined[offset : offset + length].astype(jnp.float32)
    return jax.nn.silu(summed)


def unit_rows(matrix):
    return matrix * lax.rsqrt(jnp.sum(matrix * matrix, axis=-1, keepdims=True) + norm_eps)


def unit_lower_inverse(strict, row_ids, col_ids):
    length = strict.shape[-1]
    eye = (row_ids == col_ids).astype(jnp.float32)
    inverse = eye - jnp.where(row_ids // 2 == col_ids // 2, strict, 0.0)

    def level(depth, inverse):
        width = 2 << depth
        lower_left = jnp.where(
            (row_ids // (2 * width) == col_ids // (2 * width)) & (row_ids // width != col_ids // width),
            strict,
            0.0,
        )
        return inverse - matmul_pair(matmul_pair(inverse, lower_left, highest), inverse, highest)

    return lax.fori_loop(0, length.bit_length() - 2, level, inverse)


def group_terms(query, keys, values, beta, logdecay):
    length = logdecay.shape[-1]
    cumul = jnp.cumsum(logdecay, axis=-1)
    row_ids = lax.broadcasted_iota(jnp.int32, (length, length), 0)
    col_ids = lax.broadcasted_iota(jnp.int32, (length, length), 1)
    inside = col_ids <= row_ids
    differ = cumul[..., :, None] - cumul[..., None, :]
    decay_mask = jnp.where(inside, jnp.exp(jnp.where(inside, differ, 0.0)), 0.0)
    grams = jnp.einsum(
        "...ik,...jk->...ij", jnp.concatenate([keys, query], axis=-2), keys, precision=highest
    )
    keygram = grams[..., :length, :]
    strict = jnp.where(col_ids < row_ids, beta[..., :, None] * keygram * decay_mask, 0.0)
    inverse = unit_lower_inverse(strict, row_ids, col_ids)
    updates = jnp.einsum(
        "...ij,...jd->...id",
        inverse,
        jnp.concatenate([beta[..., None] * values, (beta * jnp.exp(cumul))[..., None] * keys], axis=-1),
        precision=high,
    )
    upd_values = updates[..., : values.shape[-1]]
    upd_keys = updates[..., values.shape[-1] :]
    scores = grams[..., length:, :] * decay_mask
    last_log = cumul[..., -1:]
    query_decay = query * jnp.exp(cumul)[..., None]
    key_decay = keys * jnp.exp(last_log - cumul)[..., None]
    return (upd_values, upd_keys, scores, query_decay, key_decay, last_log[..., 0])


def group_step(state, terms):
    upd_values, upd_keys, scores, query_decay, key_decay, last_log = terms
    new_values = upd_values - jnp.einsum("...ik,...kd->...id", upd_keys, state, precision=highest)
    output = jnp.einsum("...ik,...kd->...id", query_decay, state, precision=highest)
    output = output + jnp.einsum("...ij,...jd->...id", scores, new_values, precision=highest)
    state = jnp.exp(last_log)[..., None, None] * state + jnp.einsum(
        "...ik,...id->...kd", key_decay, new_values, precision=highest
    )
    return (state, output)


def matmul_pair(left_mats, right_mats, precision=high):
    return jnp.einsum("...ij,...jk->...ik", left_mats, right_mats, precision=precision)


def body(
    query_in,
    key_in,
    value_in,
    query_taps,
    key_taps,
    value_taps,
    log_decay,
    beta_logit,
    gate_in,
    norm_gain,
):
    head_size = norm_gain.shape[0]
    length = query_in.shape[0]
    value_heads = log_decay.shape[0]
    key_heads = query_in.shape[1] // head_size
    share_ratio = value_heads // key_heads
    rim_width = query_taps.shape[0] - 1
    groups_dev = length // GROUP
    query_width, key_width = query_in.shape[1], key_in.shape[1]
    tails = shifted(
        jnp.concatenate(
            [query_in[length - rim_width :], key_in[length - rim_width :], value_in[length - rim_width :]],
            axis=1,
        ),
        "ctx",
        1,
    )
    tail_rows = (
        tails[:, :query_width],
        tails[:, query_width : query_width + key_width],
        tails[:, query_width + key_width :],
    )
    query_conv = causal_conv(jnp.concatenate([tail_rows[0], query_in], axis=0), query_taps, length)
    key_conv = causal_conv(jnp.concatenate([tail_rows[1], key_in], axis=0), key_taps, length)
    value_conv = causal_conv(jnp.concatenate([tail_rows[2], value_in], axis=0), value_taps, length)
    queries = (
        unit_rows(query_conv.reshape(length, key_heads, head_size)) * head_size ** (-0.5)
    ).astype(jnp.bfloat16)
    keys = unit_rows(key_conv.reshape(length, key_heads, head_size)).astype(jnp.bfloat16)
    values = value_conv.reshape(length, value_heads, head_size).astype(jnp.bfloat16)

    def blocked(array):
        return (
            array.astype(jnp.float32)
            .reshape(groups_dev, GROUP, array.shape[1], head_size)
            .transpose(0, 2, 1, 3)
        )

    def blocked_rates(array):
        return array.reshape(value_heads, groups_dev, GROUP).transpose(1, 0, 2)

    query_blocks = blocked(jnp.repeat(queries, share_ratio, axis=1))
    key_blocks = blocked(jnp.repeat(keys, share_ratio, axis=1))
    value_blocks = blocked(values)
    beta_blocks = blocked_rates(jax.nn.sigmoid(beta_logit))
    decay_blocks = blocked_rates(log_decay)
    terms = group_terms(query_blocks, key_blocks, value_blocks, beta_blocks, decay_blocks)
    upd_values, upd_keys, scores, query_decay, key_decay, last_log = terms
    identity_state = jnp.broadcast_to(
        jnp.eye(head_size, dtype=jnp.float32), (value_heads, head_size, head_size)
    )
    map_terms = jnp.einsum(
        "...ik,...ij->...kj", key_decay, jnp.concatenate([upd_keys, upd_values], axis=-1), precision=high
    )
    group_maps = jnp.exp(last_log)[..., None, None] * identity_state - map_terms[..., :head_size]
    group_offsets = map_terms[..., head_size:]
    score_terms = matmul_pair(scores, jnp.concatenate([upd_keys, upd_values], axis=-1))
    query_effect = query_decay - score_terms[..., :head_size]
    zero_state = jnp.zeros((value_heads, head_size, head_size), jnp.float32)
    unit_span = jnp.concatenate([identity_state, zero_state], axis=-1)

    def compose(later, earlier):
        product = matmul_pair(later[..., :head_size], earlier)
        return product + jnp.concatenate([jnp.zeros_like(later[..., :head_size]), later[..., head_size:]], axis=-1)

    spans = jnp.concatenate([group_maps, group_offsets], axis=-1)
    reach = 1
    while reach < groups_dev:
        prior = jnp.concatenate(
            [jnp.broadcast_to(unit_span, (reach,) + unit_span.shape), spans[: groups_dev - reach]]
        )
        spans = compose(spans, prior)
        reach *= 2
    shard_map_mat, local_state = spans[-1][..., :head_size], spans[-1][..., head_size:]
    entry_terms = matmul_pair(query_effect, jnp.concatenate([unit_span[None], spans[:-1]]))
    state_effect = entry_terms[..., :head_size]
    local_out = entry_terms[..., head_size:] + score_terms[..., head_size:]

    ctx_count = lax.axis_size("ctx")
    span_map, span_state = shard_map_mat, local_state
    reach = 1
    while reach < ctx_count:
        if 2 * reach < ctx_count:
            prior_map, prior_state = shifted((span_map, span_state), "ctx", reach)
            joined = matmul_pair(span_map, jnp.concatenate([prior_map, prior_state], axis=-1))
            span_state = joined[..., head_size:] + span_state
            span_map = joined[..., :head_size]
        else:
            prior_state = shifted(span_state, "ctx", reach)
            span_state = matmul_pair(span_map, prior_state) + span_state
        reach *= 2
    incoming = shifted(span_state, "ctx", 1)

    carried_out = jnp.einsum("ghik,hkd->ghid", state_effect, incoming, precision=high)
    output = (local_out + carried_out).transpose(0, 2, 1, 3).reshape(length, value_heads, head_size)
    gates = gate_in.reshape(length, value_heads, head_size).astype(jnp.float32)
    normed = (
        output
        * lax.rsqrt(jnp.mean(output * output, axis=-1, keepdims=True) + norm_eps)
        * norm_gain
        * jax.nn.silu(gates)
    )
    normed = normed.astype(jnp.bfloat16).reshape(length, value_heads * head_size)
    return lax.all_to_all(normed, "head", split_axis=0, concat_axis=1, tiled=True)


def solution(mesh):
    in_specs = (
        P("ctx", "head"),
        P("ctx", "head"),
        P("ctx", "head"),
        P(None, "head"),
        P(None, "head"),
        P(None, "head"),
        P("head", "ctx"),
        P("head", "ctx"),
        P("ctx", "head"),
        P(),
    )
    out_specs = P(("ctx", "head"), None)
    return jax.shard_map(body, mesh=mesh, in_specs=in_specs, out_specs=out_specs, check_vma=False)
```
